512 devices in a mesh: dp: 32 (over y, z_lo), ctx: 16 (over z_hi, x, core).
Axes of the slice: x: 4, y: 8, z: 8 (z_hi: 2, z_lo: 4; z = z_hi * 4 + z_lo), core: 2. Of those that a mesh axis runs over, the one named last changes fastest.
Arguments:
- projected: bfloat16 [2, 32, 2048, 4096], P(None, 'dp', 'ctx'), may hold values from -6 to 6
- token_ids: int32 [32, 2048], P('dp', 'ctx'), may hold values from 0 to 511
- short_filters: float32 [2, 7, 4096], P(None, None, 'ctx'), may hold values from -2 to 2
- medium_filter: bfloat16 [128, 4096], P(None, 'ctx'), may hold values from -0.75 to 0.75
- skip_gain: float32 [4096], P('ctx'), may hold values from -3 to 3
Outputs:
- grad_projected: bfloat16 [2, 32, 2048, 4096], P(None, 'dp', 'ctx')
- grad_short: float32 [2, 7, 4096], P(None, None, 'ctx')
- grad_medium: float32 [128, 4096], P(None, 'ctx')
- grad_skip: float32 [4096], P('ctx')
The draws below stay inside these ranges and needn't reach their ends.
All inputs are finite; a program needn't handle non-finite values.
Results may differ from the reference program's by a relative error of at most 0.024.
Values may be sent and summed in bfloat16 or wider, within the bound.
No kernel may reach another device: no remote copies, remote signals or barrier semaphores. Data moves between devices by JAX's collectives and lax.ppermute only.
A program may use at most 128 MiB of HBM per device.

```python
import jax
import jax.numpy as jnp
from jax import lax

C = 4096
FILT = 128
SHORT = 7
SEQS = 32
LEN = 2048


def with_ends(array, own_key, least, top_value):
    place = [jax.random.randint(jax.random.fold_in(own_key, axis), (), 0, length) for axis, length in enumerate(array.shape)]
    main_axis = array.shape.index(max(array.shape))
    beside = place[:main_axis] + [(place[main_axis] + 1) % array.shape[main_axis]] + place[main_axis + 1:]
    return array.at[tuple(place)].set(least).at[tuple(beside)].set(top_value)


def block_levels(own_key, extent, shards, smallest, largest):
    level = 1.0
    for axis_at, parts in shards:
        draws = jax.random.uniform(jax.random.fold_in(jax.random.fold_in(own_key, 6), axis_at), (parts,), jnp.float32, smallest / len(shards), largest / len(shards))
        level = level * jnp.repeat(jnp.exp(draws), extent[axis_at] // parts).reshape((-1,) + (1,) * (len(extent) - 1 - axis_at))
    return level


def scatter_about(rng, dims, deviation, most, cuts=(), dtype=jnp.bfloat16):
    loudness = block_levels(rng, dims, cuts, -0.22, 0.18) if cuts else 1.0
    array = jax.random.normal(rng, dims, jnp.float32) * deviation * loudness
    return jnp.minimum(jnp.maximum(array, -most), most).astype(dtype)


def setup_inputs(seed: int = 0) -> dict:
    streams_of = jax.random.split(jax.random.key(seed), 6)
    projected = scatter_about(streams_of[0], (2, SEQS, LEN, C), 1.0, 6.0, ((1, 32), (2, 16)))
    token_ids = with_ends(jax.random.randint(streams_of[1], (SEQS, LEN), 0, 512), jax.random.fold_in(streams_of[1], 1), 0, 511).astype(jnp.int32)
    short_filters = scatter_about(streams_of[2], (2, SHORT, C), SHORT ** -0.5, 2.0, ((2, 16),), jnp.float32)
    medium_filter = scatter_about(streams_of[3], (FILT, C), (FILT // 2) ** -0.5, 0.75, ((1, 16),))
    skip_gain = scatter_about(streams_of[4], (C,), 0.5, 3.0, ((0, 16),), jnp.float32)
    return dict(projected=projected, token_ids=token_ids, short_filters=short_filters, medium_filter=medium_filter, skip_gain=skip_gain)


def short_forward(extended, filters):
    short_len = filters.shape[1]
    length = extended.shape[1] - short_len + 1
    result = jnp.zeros((extended.shape[0], length, extended.shape[2]), jnp.float32)
    for offset in range(short_len):
        start = short_len - 1 - offset
        result = result + filters[:, offset][:, None, :] * extended[:, start:start + length].astype(jnp.float32)
    return result


def short_backward(extended, filters):
    short_len = filters.shape[1]
    length = extended.shape[1] - short_len + 1
    result = jnp.zeros((extended.shape[0], length, extended.shape[2]), jnp.float32)
    for offset in range(short_len):
        result = result + filters[:, offset][:, None, :] * extended[:, offset:offset + length].astype(jnp.float32)
    return result


def short_weights(grads, extended):
    short_len = extended.shape[1] - grads.shape[1] + 1
    length = grads.shape[1]
    rows = []
    for offset in range(short_len):
        start = short_len - 1 - offset
        rows.append(jnp.sum(grads.astype(jnp.float32) * extended[:, start:start + length].astype(jnp.float32), axis=1))
    return jnp.stack(rows, axis=1)


def causal_fft(signal, kernel):
    length = signal.shape[0]
    total = length + kernel.shape[0]
    spectrum = jnp.fft.rfft(signal, n=total, axis=0) * jnp.fft.rfft(kernel, n=total, axis=0)
    return jnp.fft.irfft(spectrum, n=total, axis=0)[:length]


def anti_fft(signal, kernel):
    length = signal.shape[0]
    total = length + kernel.shape[0]
    spectrum = jnp.conj(jnp.fft.rfft(kernel, n=total, axis=0)) * jnp.fft.rfft(signal, n=total, axis=0)
    return jnp.fft.irfft(spectrum, n=total, axis=0)[:length]


def lag_fft(later, earlier, taps):
    total = later.shape[0] + taps
    spectrum = jnp.conj(jnp.fft.rfft(earlier, n=total, axis=0)) * jnp.fft.rfft(later, n=total, axis=0)
    return jnp.fft.irfft(spectrum, n=total, axis=0)[:taps]


def reference(projected, token_ids, short_filters, medium_filter, skip_gain):
    short_len = short_filters.shape[1]
    filter_len = medium_filter.shape[0]
    medium = medium_filter.astype(jnp.float32)

    def one_sequence(items):
        inputs, idents = items
        loss_weight = jnp.where((idents >= 97) & (idents <= 122), 0.1, 1.0).astype(jnp.bfloat16)
        padded_inputs = jnp.pad(inputs, ((0, 0), (short_len - 1, 0), (0, 0)))
        filtered = short_forward(padded_inputs, short_filters)
        product = (filtered[0] * filtered[1]).astype(jnp.bfloat16)
        product_f = product.astype(jnp.float32)
        mix = causal_fft(product_f, medium) + skip_gain * product_f
        grad_mix = (loss_weight.astype(jnp.float32)[:, None] * mix).astype(jnp.bfloat16)
        grad_mix_f = grad_mix.astype(jnp.float32)
        back_product = anti_fft(grad_mix_f, medium) + skip_gain * grad_mix_f
        grad_key = (back_product * filtered[1]).astype(jnp.bfloat16)
        grad_value = (back_product * filtered[0]).astype(jnp.bfloat16)
        grad_filtered = jnp.stack([grad_key, grad_value])
        padded_grads = jnp.pad(grad_filtered, ((0, 0), (0, short_len - 1), (0, 0)))
        grad_inputs = short_backward(padded_grads, short_filters).astype(jnp.bfloat16)
        grad_taps = lag_fft(grad_mix_f, product_f, filter_len)
        grad_gain = jnp.sum(grad_mix_f * product_f, axis=0)
        grad_short = short_weights(grad_filtered, padded_inputs)
        return grad_inputs, grad_short, grad_taps, grad_gain

    results = lax.map(one_sequence, (jnp.moveaxis(projected, 1, 0), token_ids))
    grad_projected = jnp.moveaxis(results[0], 0, 1)
    grad_short = jnp.sum(results[1], axis=0) / SEQS
    grad_medium = jnp.sum(results[2], axis=0) / SEQS
    grad_skip = jnp.sum(results[3], axis=0) / SEQS
    return grad_projected, grad_short, grad_medium, grad_skip
```

```python
import jax
import jax.numpy as jnp
from jax import lax
from jax.sharding import PartitionSpec as P


def short_forward(extended, filters):
    short_len = filters.shape[1]
    length = extended.shape[1] - short_len + 1
    result = jnp.zeros((extended.shape[0], length, extended.shape[2]), jnp.float32)
    for offset in range(short_len):
        start = short_len - 1 - offset
        result = result + filters[:, offset][:, None, :] * extended[
            :, start : start + length
        ].astype(jnp.float32)
    return result


def short_backward(extended, filters):
    short_len = filters.shape[1]
    length = extended.shape[1] - short_len + 1
    result = jnp.zeros((extended.shape[0], length, extended.shape[2]), jnp.float32)
    for offset in range(short_len):
        result = result + filters[:, offset][:, None, :] * extended[
            :, offset : offset + length
        ].astype(jnp.float32)
    return result


def short_weights(grads, extended):
    short_len = extended.shape[1] - grads.shape[1] + 1
    length = grads.shape[1]
    rows = []
    for offset in range(short_len):
        start = short_len - 1 - offset
        rows.append(
            jnp.sum(
                grads.astype(jnp.float32) * extended[:, start : start + length].astype(jnp.float32),
                axis=1,
            )
        )
    return jnp.stack(rows, axis=1)


def depthwise(extended, kernel):
    result = lax.conv_general_dilated(
        extended[None],
        kernel[:, None, :],
        (1,),
        "VALID",
        dimension_numbers=("NWC", "WIO", "NWC"),
        feature_group_count=extended.shape[1],
        preferred_element_type=jnp.float32,
    )
    return result[0]


def butterfly_sum(value, axis, size):
    bit = 1
    while bit < size:
        perm = [(i, i ^ bit) for i in range(size)]
        value = value + lax.ppermute(value, axis, perm)
        bit *= 2
    return value


def local(projected, token_ids, short_filters, medium_filter, skip_gain):
    inputs = projected[:, 0]
    short_len = short_filters.shape[1]
    filter_len = medium_filter.shape[0]
    length = inputs.shape[1]
    groups = lax.axis_size("dp")
    shards = lax.axis_size("ctx")
    loss_weight = jnp.where((token_ids[0] >= 97) & (token_ids[0] <= 122), 0.1, 1.0).astype(
        jnp.bfloat16
    )
    weight_rows = jnp.broadcast_to(loss_weight[None, :, None], (1, length, shards))
    all_inputs, all_weight = (
        lax.all_to_all(inputs, "ctx", split_axis=2, concat_axis=1, tiled=True),
        lax.all_to_all(weight_rows, "ctx", split_axis=2, concat_axis=1, tiled=True),
    )
    weight_seq = all_weight[0, :, 0].astype(jnp.float32)
    padded_inputs = jnp.pad(all_inputs, ((0, 0), (short_len - 1, 0), (0, 0)))
    filtered = short_forward(padded_inputs, short_filters)
    product = (filtered[0] * filtered[1]).astype(jnp.bfloat16)
    padded_product = jnp.pad(product, ((filter_len - 1, 0), (0, 0)))
    mix = depthwise(padded_product, medium_filter[::-1]) + skip_gain * product.astype(jnp.float32)
    grad_mix = (weight_seq[:, None] * mix).astype(jnp.bfloat16)
    padded_later = jnp.pad(grad_mix, ((0, filter_len - 1), (0, 0)))
    back_product = depthwise(padded_later, medium_filter) + skip_gain * grad_mix.astype(jnp.float32)
    grad_key = (back_product * filtered[1]).astype(jnp.bfloat16)
    grad_value = (back_product * filtered[0]).astype(jnp.bfloat16)
    grad_filtered = jnp.stack([grad_key, grad_value])
    padded_grads = jnp.pad(grad_filtered, ((0, 0), (0, short_len - 1), (0, 0)))
    grad_channels = short_backward(padded_grads, short_filters).astype(jnp.bfloat16)
    grad_inputs = lax.all_to_all(grad_channels, "ctx", split_axis=1, concat_axis=2, tiled=True)
    grad_taps = depthwise(padded_product, grad_mix)[::-1]
    grad_gain = jnp.sum(grad_mix.astype(jnp.float32) * product.astype(jnp.float32), axis=0)
    grad_short = short_weights(grad_filtered, padded_inputs)
    taps = grad_taps.shape[0]
    stacked = jnp.concatenate(
        [grad_taps, grad_short.reshape(-1, grad_short.shape[-1]), grad_gain[None]], axis=0
    ).astype(jnp.float32)
    stacked = butterfly_sum(stacked, "dp", groups)
    grad_taps = stacked[:taps]
    grad_short = stacked[taps : taps + grad_short.shape[0] * short_len].reshape(grad_short.shape)
    grad_gain = stacked[-1]
    return (grad_inputs[:, None], grad_short / groups, grad_taps / groups, grad_gain / groups)


def solution(mesh):
    placed = (
        P(None, "dp", "ctx", None),
        P("dp", "ctx"),
        P(None, None, "ctx"),
        P(None, "ctx"),
        P("ctx"),
    )
    return jax.shard_map(
        local,
        mesh=mesh,
        in_specs=placed,
        out_specs=(P(None, "dp", "ctx", None), P(None, None, "ctx"), P(None, "ctx"), P("ctx")),
        check_vma=False,
    )
```

```python
import jax
import jax.numpy as jnp
from jax import lax
from jax.sharding import PartitionSpec as P


def short_forward(extended, filters):
    short_len = filters.shape[1]
    length = extended.shape[1] - short_len + 1
    result = jnp.zeros((extended.shape[0], length, extended.shape[2]), jnp.float32)
    for offset in range(short_len):
        start = short_len - 1 - offset
        result = result + filters[:, offset][:, None, :] * extended[
            :, start : start + length
        ].astype(jnp.float32)
    return result


def short_backward(extended, filters):
    short_len = filters.shape[1]
    length = extended.shape[1] - short_len + 1
    result = jnp.zeros((extended.shape[0], length, extended.shape[2]), jnp.float32)
    for offset in range(short_len):
        result = result + filters[:, offset][:, None, :] * extended[
            :, offset : offset + length
        ].astype(jnp.float32)
    return result


def short_weights(grads, extended):
    short_len = extended.shape[1] - grads.shape[1] + 1
    length = grads.shape[1]
    rows = []
    for offset in range(short_len):
        start = short_len - 1 - offset
        rows.append(
            jnp.sum(
                grads.astype(jnp.float32) * extended[:, start : start + length].astype(jnp.float32),
                axis=1,
            )
        )
    return jnp.stack(rows, axis=1)


def depthwise(extended, kernel):
    result = lax.conv_general_dilated(
        extended[None],
        kernel[:, None, :],
        (1,),
        "VALID",
        dimension_numbers=("NWC", "WIO", "NWC"),
        feature_group_count=extended.shape[1],
        preferred_element_type=jnp.float32,
    )
    return result[0]


def butterfly_sum(value, axis, size):
    bit = 1
    while bit < size:
        perm = [(i, i ^ bit) for i in range(size)]
        value = value + lax.ppermute(value, axis, perm)
        bit *= 2
    return value


def local(projected, token_ids, short_filters, medium_filter, skip_gain):
    inputs = projected[:, 0]
    short_len = short_filters.shape[1]
    filter_len = medium_filter.shape[0]
    length = inputs.shape[1]
    groups = lax.axis_size("dp")
    shards = lax.axis_size("ctx")
    all_inputs = lax.all_to_all(inputs, "ctx", split_axis=2, concat_axis=1, tiled=True)
    all_ids = lax.all_gather(token_ids[0], "ctx", tiled=True)
    weight_seq = (
        jnp.where((all_ids >= 97) & (all_ids <= 122), 0.1, 1.0)
        .astype(jnp.bfloat16)
        .astype(jnp.float32)
    )
    padded_inputs = jnp.pad(all_inputs, ((0, 0), (short_len - 1, 0), (0, 0)))
    filtered = short_forward(padded_inputs, short_filters)
    product = (filtered[0] * filtered[1]).astype(jnp.bfloat16)
    padded_product = jnp.pad(product, ((filter_len - 1, 0), (0, 0)))
    mix = depthwise(padded_product, medium_filter[::-1]) + skip_gain * product.astype(jnp.float32)
    grad_mix = (weight_seq[:, None] * mix).astype(jnp.bfloat16)
    grad_taps = depthwise(padded_product, grad_mix)[::-1]
    grad_gain = jnp.sum(grad_mix.astype(jnp.float32) * product.astype(jnp.float32), axis=0)
    taps = grad_taps.shape[0]
    stacked = jnp.concatenate([grad_taps, grad_gain[None]], axis=0).astype(jnp.float32)
    stacked = butterfly_sum(stacked, "dp", groups)
    grad_taps = stacked[:taps]
    grad_gain = stacked[taps]
    padded_later = jnp.pad(grad_mix, ((0, filter_len - 1), (0, 0)))
    back_product = depthwise(padded_later, medium_filter) + skip_gain * grad_mix.astype(jnp.float32)
    grad_key = (back_product * filtered[1]).astype(jnp.bfloat16)
    grad_value = (back_product * filtered[0]).astype(jnp.bfloat16)
    grad_filtered = jnp.stack([grad_key, grad_value])
    padded_grads = jnp.pad(grad_filtered, ((0, 0), (0, short_len - 1), (0, 0)))
    grad_channels = short_backward(padded_grads, short_filters).astype(jnp.bfloat16)
    grad_inputs = lax.all_to_all(grad_channels, "ctx", split_axis=1, concat_axis=2, tiled=True)
    grad_short = short_weights(grad_filtered, padded_inputs)
    grad_short = butterfly_sum(grad_short.astype(jnp.float32), "dp", groups)
    return (grad_inputs[:, None], grad_short / groups, grad_taps / groups, grad_gain / groups)


def solution(mesh):
    placed = (
        P(None, "dp", "ctx", None),
        P("dp", "ctx"),
        P(None, None, "ctx"),
        P(None, "ctx"),
        P("ctx"),
    )
    return jax.shard_map(
        local,
        mesh=mesh,
        in_specs=placed,
        out_specs=(P(None, "dp", "ctx", None), P(None, None, "ctx"), P(None, "ctx"), P("ctx")),
        check_vma=False,
    )
```

```python
import jax
import jax.numpy as jnp
from jax import lax
from jax.sharding import PartitionSpec as P


def short_forward(extended, filters):
    short_len = filters.shape[1]
    length = extended.shape[1] - short_len + 1
    result = jnp.zeros((extended.shape[0], length, extended.shape[2]), jnp.float32)
    for offset in range(short_len):
        start = short_len - 1 - offset
        result = result + filters[:, offset][:, None, :] * extended[
            :, start : start + length
        ].astype(jnp.float32)
    return result


def short_backward(extended, filters):
    short_len = filters.shape[1]
    length = extended.shape[1] - short_len + 1
    result = jnp.zeros((extended.shape[0], length, extended.shape[2]), jnp.float32)
    for offset in range(short_len):
        result = result + filters[:, offset][:, None, :] * extended[
            :, offset : offset + length
        ].astype(jnp.float32)
    return result


def short_weights(grads, extended):
    short_len = extended.shape[1] - grads.shape[1] + 1
    length = grads.shape[1]
    rows = []
    for offset in range(short_len):
        start = short_len - 1 - offset
        rows.append(
            jnp.sum(
                grads.astype(jnp.float32) * extended[:, start : start + length].astype(jnp.float32),
                axis=1,
            )
        )
    return jnp.stack(rows, axis=1)


def depthwise(extended, kernel):
    result = lax.conv_general_dilated(
        extended[None],
        kernel[:, None, :],
        (1,),
        "VALID",
        dimension_numbers=("NWC", "WIO", "NWC"),
        feature_group_count=extended.shape[1],
        preferred_element_type=jnp.float32,
    )
    return result[0]


def butterfly_sum(value, axis, size):
    bit = 1
    while bit < size:
        perm = [(i, i ^ bit) for i in range(size)]
        value = value + lax.ppermute(value, axis, perm)
        bit *= 2
    return value


def exchange_sum(value, axis, size):
    rows = value.shape[0]
    piece = -(-rows // size)
    padded = jnp.pad(value, ((0, piece * size - rows), (0, 0))).reshape(size, piece, -1)
    received = lax.all_to_all(padded, axis, split_axis=0, concat_axis=0, tiled=True)
    reduced = jnp.sum(received, axis=0)
    spread = jnp.broadcast_to(reduced[None], (size,) + reduced.shape)
    gathered = lax.all_to_all(spread, axis, split_axis=0, concat_axis=0, tiled=True)
    return gathered.reshape(size * piece, -1)[:rows]


def local(projected, token_ids, short_filters, medium_filter, skip_gain):
    inputs = projected[:, 0]
    short_len = short_filters.shape[1]
    filter_len = medium_filter.shape[0]
    length = inputs.shape[1]
    groups = lax.axis_size("dp")
    shards = lax.axis_size("ctx")
    loss_weight = jnp.where((token_ids[0] >= 97) & (token_ids[0] <= 122), 0.1, 1.0).astype(
        jnp.bfloat16
    )
    weight_rows = jnp.broadcast_to(loss_weight[None, :, None], (1, length, shards))
    all_inputs, all_weight = (
        lax.all_to_all(inputs, "ctx", split_axis=2, concat_axis=1, tiled=True),
        lax.all_to_all(weight_rows, "ctx", split_axis=2, concat_axis=1, tiled=True),
    )
    weight_seq = all_weight[0, :, 0].astype(jnp.float32)
    padded_inputs = jnp.pad(all_inputs, ((0, 0), (short_len - 1, 0), (0, 0)))
    filtered = short_forward(padded_inputs, short_filters)
    product = (filtered[0] * filtered[1]).astype(jnp.bfloat16)
    padded_product = jnp.pad(product, ((filter_len - 1, 0), (0, 0)))
    mix = depthwise(padded_product, medium_filter[::-1]) + skip_gain * product.astype(jnp.float32)
    grad_mix = (weight_seq[:, None] * mix).astype(jnp.bfloat16)
    padded_later = jnp.pad(grad_mix, ((0, filter_len - 1), (0, 0)))
    back_product = depthwise(padded_later, medium_filter) + skip_gain * grad_mix.astype(jnp.float32)
    grad_key = (back_product * filtered[1]).astype(jnp.bfloat16)
    grad_value = (back_product * filtered[0]).astype(jnp.bfloat16)
    grad_filtered = jnp.stack([grad_key, grad_value])
    padded_grads = jnp.pad(grad_filtered, ((0, 0), (0, short_len - 1), (0, 0)))
    grad_channels = short_backward(padded_grads, short_filters).astype(jnp.bfloat16)
    grad_inputs = lax.all_to_all(grad_channels, "ctx", split_axis=1, concat_axis=2, tiled=True)
    grad_taps = depthwise(padded_product, grad_mix)[::-1]
    grad_gain = jnp.sum(grad_mix.astype(jnp.float32) * product.astype(jnp.float32), axis=0)
    grad_short = short_weights(grad_filtered, padded_inputs)
    taps = grad_taps.shape[0]
    stacked = jnp.concatenate(
        [grad_taps, grad_short.reshape(-1, grad_short.shape[-1]), grad_gain[None]], axis=0
    ).astype(jnp.float32)
    stacked = exchange_sum(stacked, "dp", groups)
    grad_taps = stacked[:taps]
    grad_short = stacked[taps : taps + grad_short.shape[0] * short_len].reshape(grad_short.shape)
    grad_gain = stacked[-1]
    return (grad_inputs[:, None], grad_short / groups, grad_taps / groups, grad_gain / groups)


def solution(mesh):
    placed = (
        P(None, "dp", "ctx", None),
        P("dp", "ctx"),
        P(None, None, "ctx"),
        P(None, "ctx"),
        P("ctx"),
    )
    return jax.shard_map(
        local,
        mesh=mesh,
        in_specs=placed,
        out_specs=(P(None, "dp", "ctx", None), P(None, None, "ctx"), P(None, "ctx"), P("ctx")),
        check_vma=False,
    )
```

```python
import jax
import jax.numpy as jnp
from jax import lax
from jax.sharding import PartitionSpec as P


def short_forward(extended, filters):
    short_len = filters.shape[1]
    length = extended.shape[1] - short_len + 1
    result = jnp.zeros((extended.shape[0], length, extended.shape[2]), jnp.float32)
    for offset in range(short_len):
        start = short_len - 1 - offset
        result = result + filters[:, offset][:, None, :] * extended[
            :, start : start + length
        ].astype(jnp.float32)
    return result


def short_backward(extended, filters):
    short_len = filters.shape[1]
    length = extended.shape[1] - short_len + 1
    result = jnp.zeros((extended.shape[0], length, extended.shape[2]), jnp.float32)
    for offset in range(short_len):
        result = result + filters[:, offset][:, None, :] * extended[
            :, offset : offset + length
        ].astype(jnp.float32)
    return result


def short_weights(grads, extended):
    short_len = extended.shape[1] - grads.shape[1] + 1
    length = grads.shape[1]
    rows = []
    for offset in range(short_len):
        start = short_len - 1 - offset
        rows.append(
            jnp.sum(
                grads.astype(jnp.float32) * extended[:, start : start + length].astype(jnp.float32),
                axis=1,
            )
        )
    return jnp.stack(rows, axis=1)


def depthwise(extended, kernel):
    result = lax.conv_general_dilated(
        extended[None],
        kernel[:, None, :],
        (1,),
        "VALID",
        dimension_numbers=("NWC", "WIO", "NWC"),
        feature_group_count=extended.shape[1],
        preferred_element_type=jnp.float32,
    )
    return result[0]


def butterfly_sum(value, axis, size):
    bit = 1
    while bit < size:
        perm = [(i, i ^ bit) for i in range(size)]
        value = value + lax.ppermute(value, axis, perm)
        bit *= 2
    return value


def local(projected, token_ids, short_filters, medium_filter, skip_gain):
    inputs = projected[:, 0]
    short_len = short_filters.shape[1]
    filter_len = medium_filter.shape[0]
    length = inputs.shape[1]
    groups = lax.axis_size("dp")
    shards = lax.axis_size("ctx")
    loss_weight = jnp.where((token_ids[0] >= 97) & (token_ids[0] <= 122), 0.1, 1.0).astype(
        jnp.bfloat16
    )
    weight_rows = jnp.broadcast_to(loss_weight[None, :, None], (1, length, shards))
    all_inputs, all_weight = (
        lax.all_to_all(inputs, "ctx", split_axis=2, concat_axis=1, tiled=True),
        lax.all_to_all(weight_rows, "ctx", split_axis=2, concat_axis=1, tiled=True),
    )
    weight_seq = all_weight[0, :, 0].astype(jnp.float32)
    padded_inputs = jnp.pad(all_inputs, ((0, 0), (short_len - 1, 0), (0, 0)))
    filtered = short_forward(padded_inputs, short_filters)
    product = (filtered[0] * filtered[1]).astype(jnp.bfloat16)
    padded_product = jnp.pad(product, ((filter_len - 1, 0), (0, 0)))
    mix = depthwise(padded_product, medium_filter[::-1]) + skip_gain * product.astype(jnp.float32)
    grad_mix = (weight_seq[:, None] * mix).astype(jnp.bfloat16)
    grad_taps = depthwise(padded_product, grad_mix)[::-1]
    grad_gain = jnp.sum(grad_mix.astype(jnp.float32) * product.astype(jnp.float32), axis=0)
    taps = grad_taps.shape[0]
    stacked = jnp.concatenate([grad_taps, grad_gain[None]], axis=0).astype(jnp.float32)
    stacked, grad_mix = lax.optimization_barrier((stacked, grad_mix))
    padded_later = jnp.pad(grad_mix, ((0, filter_len - 1), (0, 0)))
    pieces = 4
    span = grad_mix.shape[0] // pieces
    parts = []
    bit = 1
    for k in range(pieces):
        window = padded_later[k * span : (k + 1) * span + filter_len - 1]
        if k > 0:
            stacked = stacked + lax.ppermute(
                stacked, "dp", [(i, i ^ bit) for i in range(groups)]
            )
            bit *= 2
            stacked, window = lax.optimization_barrier((stacked, window))
        parts.append(depthwise(window, medium_filter))
    while bit < groups:
        stacked = stacked + lax.ppermute(stacked, "dp", [(i, i ^ bit) for i in range(groups)])
        bit *= 2
    grad_taps = stacked[:taps]
    grad_gain = stacked[taps]
    back_product = jnp.concatenate(parts, axis=0) + skip_gain * grad_mix.astype(jnp.float32)
    grad_key = (back_product * filtered[1]).astype(jnp.bfloat16)
    grad_value = (back_product * filtered[0]).astype(jnp.bfloat16)
    grad_filtered = jnp.stack([grad_key, grad_value])
    padded_grads = jnp.pad(grad_filtered, ((0, 0), (0, short_len - 1), (0, 0)))
    grad_channels = short_backward(padded_grads, short_filters).astype(jnp.bfloat16)
    grad_inputs = lax.all_to_all(grad_channels, "ctx", split_axis=1, concat_axis=2, tiled=True)
    grad_short = short_weights(grad_filtered, padded_inputs)
    grad_short = butterfly_sum(grad_short.astype(jnp.float32), "dp", groups)
    return (grad_inputs[:, None], grad_short / groups, grad_taps / groups, grad_gain / groups)


def solution(mesh):
    placed = (
        P(None, "dp", "ctx", None),
        P("dp", "ctx"),
        P(None, None, "ctx"),
        P(None, "ctx"),
        P("ctx"),
    )
    return jax.shard_map(
        local,
        mesh=mesh,
        in_specs=placed,
        out_specs=(P(None, "dp", "ctx", None), P(None, None, "ctx"), P(None, "ctx"), P("ctx")),
        check_vma=False,
    )
```

```python
import jax
import jax.numpy as jnp
from jax import lax
from jax.sharding import PartitionSpec as P


def short_forward(extended, filters):
    short_len = filters.shape[1]
    length = extended.shape[1] - short_len + 1
    result = jnp.zeros((extended.shape[0], length, extended.shape[2]), jnp.float32)
    for offset in range(short_len):
        start = short_len - 1 - offset
        result = result + filters[:, offset][:, None, :] * extended[
            :, start : start + length
        ].astype(jnp.float32)
    return result


def short_backward(extended, filters):
    short_len = filters.shape[1]
    length = extended.shape[1] - short_len + 1
    result = jnp.zeros((extended.shape[0], length, extended.shape[2]), jnp.float32)
    for offset in range(short_len):
        result = result + filters[:, offset][:, None, :] * extended[
            :, offset : offset + length
        ].astype(jnp.float32)
    return result


def short_weights(grads, extended):
    short_len = extended.shape[1] - grads.shape[1] + 1
    length = grads.shape[1]
    rows = []
    for offset in range(short_len):
        start = short_len - 1 - offset
        rows.append(
            jnp.sum(
                grads.astype(jnp.float32) * extended[:, start : start + length].astype(jnp.float32),
                axis=1,
            )
        )
    return jnp.stack(rows, axis=1)


def depthwise(extended, kernel):
    result = lax.conv_general_dilated(
        extended[None],
        kernel[:, None, :],
        (1,),
        "VALID",
        dimension_numbers=("NWC", "WIO", "NWC"),
        feature_group_count=extended.shape[1],
        preferred_element_type=jnp.float32,
    )
    return result[0]


def butterfly_sum(value, axis, size):
    bit = 1
    while bit < size:
        perm = [(i, i ^ bit) for i in range(size)]
        value = value + lax.ppermute(value, axis, perm)
        bit *= 2
    return value


def local(projected, token_ids, short_filters, medium_filter, skip_gain):
    inputs = projected[:, 0]
    short_len = short_filters.shape[1]
    filter_len = medium_filter.shape[0]
    length = inputs.shape[1]
    groups = lax.axis_size("dp")
    shards = lax.axis_size("ctx")
    loss_weight = jnp.where((token_ids[0] >= 97) & (token_ids[0] <= 122), 0.1, 1.0).astype(
        jnp.bfloat16
    )
    extra = 8
    width = inputs.shape[2] // shards
    weight_row = jnp.tile(jnp.pad(loss_weight, (0, width - length)), shards)
    extra_rows = jnp.zeros((2, extra, inputs.shape[2]), inputs.dtype).at[0, 0].set(weight_row)
    joined = jnp.concatenate([inputs, extra_rows], axis=1)
    received = lax.all_to_all(joined, "ctx", split_axis=2, concat_axis=1, tiled=True)
    received = received.reshape(2, shards, length + extra, width)
    all_inputs = received[:, :, :length].reshape(2, shards * length, width)
    weight_seq = received[0, :, length, :length].reshape(-1).astype(jnp.float32)
    padded_inputs = jnp.pad(all_inputs, ((0, 0), (short_len - 1, 0), (0, 0)))
    filtered = short_forward(padded_inputs, short_filters)
    product = (filtered[0] * filtered[1]).astype(jnp.bfloat16)
    padded_product = jnp.pad(product, ((filter_len - 1, 0), (0, 0)))
    mix = depthwise(padded_product, medium_filter[::-1]) + skip_gain * product.astype(jnp.float32)
    grad_mix = (weight_seq[:, None] * mix).astype(jnp.bfloat16)
    padded_later = jnp.pad(grad_mix, ((0, filter_len - 1), (0, 0)))
    back_product = depthwise(padded_later, medium_filter) + skip_gain * grad_mix.astype(jnp.float32)
    grad_key = (back_product * filtered[1]).astype(jnp.bfloat16)
    grad_value = (back_product * filtered[0]).astype(jnp.bfloat16)
    grad_filtered = jnp.stack([grad_key, grad_value])
    padded_grads = jnp.pad(grad_filtered, ((0, 0), (0, short_len - 1), (0, 0)))
    grad_channels = short_backward(padded_grads, short_filters).astype(jnp.bfloat16)
    grad_inputs = lax.all_to_all(grad_channels, "ctx", split_axis=1, concat_axis=2, tiled=True)
    grad_taps = depthwise(padded_product, grad_mix)[::-1]
    grad_gain = jnp.sum(grad_mix.astype(jnp.float32) * product.astype(jnp.float32), axis=0)
    grad_short = short_weights(grad_filtered, padded_inputs)
    taps = grad_taps.shape[0]
    stacked = jnp.concatenate(
        [grad_taps, grad_short.reshape(-1, grad_short.shape[-1]), grad_gain[None]], axis=0
    ).astype(jnp.float32)
    stacked = butterfly_sum(stacked, "dp", groups)
    grad_taps = stacked[:taps]
    grad_short = stacked[taps : taps + grad_short.shape[0] * short_len].reshape(grad_short.shape)
    grad_gain = stacked[-1]
    return (grad_inputs[:, None], grad_short / groups, grad_taps / groups, grad_gain / groups)


def solution(mesh):
    placed = (
        P(None, "dp", "ctx", None),
        P("dp", "ctx"),
        P(None, None, "ctx"),
        P(None, "ctx"),
        P("ctx"),
    )
    return jax.shard_map(
        local,
        mesh=mesh,
        in_specs=placed,
        out_specs=(P(None, "dp", "ctx", None), P(None, None, "ctx"), P(None, "ctx"), P("ctx")),
        check_vma=False,
    )
```

```python
import jax
import jax.numpy as jnp
from jax import lax
from jax.sharding import PartitionSpec as P


def short_forward(extended, filters):
    short_len = filters.shape[1]
    length = extended.shape[1] - short_len + 1
    result = jnp.zeros((extended.shape[0], length, extended.shape[2]), jnp.float32)
    for offset in range(short_len):
        start = short_len - 1 - offset
        result = result + filters[:, offset][:, None, :] * extended[
            :, start : start + length
        ].astype(jnp.float32)
    return result


def short_backward(extended, filters):
    short_len = filters.shape[1]
    length = extended.shape[1] - short_len + 1
    result = jnp.zeros((extended.shape[0], length, extended.shape[2]), jnp.float32)
    for offset in range(short_len):
        result = result + filters[:, offset][:, None, :] * extended[
            :, offset : offset + length
        ].astype(jnp.float32)
    return result


def short_weights(grads, extended):
    short_len = extended.shape[1] - grads.shape[1] + 1
    length = grads.shape[1]
    rows = []
    for offset in range(short_len):
        start = short_len - 1 - offset
        rows.append(
            jnp.sum(
                grads.astype(jnp.float32) * extended[:, start : start + length].astype(jnp.float32),
                axis=1,
            )
        )
    return jnp.stack(rows, axis=1)


def depthwise(extended, kernel):
    result = lax.conv_general_dilated(
        extended[None],
        kernel[:, None, :],
        (1,),
        "VALID",
        dimension_numbers=("NWC", "WIO", "NWC"),
        feature_group_count=extended.shape[1],
        preferred_element_type=jnp.float32,
    )
    return result[0]


def butterfly_sum(value, axis, size):
    bit = 1
    while bit < size:
        perm = [(i, i ^ bit) for i in range(size)]
        value = value + lax.ppermute(value, axis, perm)
        bit *= 2
    return value


def grouped_sum(value, axis, size, inner):
    index = lax.axis_index(axis)
    for stride, count in ((1, inner), (inner, size // inner)):
        rank = (index // stride) % count
        received = [value]
        for shift in range(1, count):
            perm = [
                (i, i + (((i // stride) % count + shift) % count - (i // stride) % count) * stride)
                for i in range(size)
            ]
            received.append(lax.ppermute(value, axis, perm))
        order = (rank - jnp.arange(count)) % count
        ranked = jnp.take(jnp.stack(received), order, axis=0)
        value = ranked[0]
        for k in range(1, count):
            value = value + ranked[k]
    return value


def local(projected, token_ids, short_filters, medium_filter, skip_gain):
    inputs = projected[:, 0]
    short_len = short_filters.shape[1]
    filter_len = medium_filter.shape[0]
    length = inputs.shape[1]
    groups = lax.axis_size("dp")
    shards = lax.axis_size("ctx")
    loss_weight = jnp.where((token_ids[0] >= 97) & (token_ids[0] <= 122), 0.1, 1.0).astype(
        jnp.bfloat16
    )
    weight_rows = jnp.broadcast_to(loss_weight[None, :, None], (1, length, shards))
    all_inputs, all_weight = (
        lax.all_to_all(inputs, "ctx", split_axis=2, concat_axis=1, tiled=True),
        lax.all_to_all(weight_rows, "ctx", split_axis=2, concat_axis=1, tiled=True),
    )
    weight_seq = all_weight[0, :, 0].astype(jnp.float32)
    padded_inputs = jnp.pad(all_inputs, ((0, 0), (short_len - 1, 0), (0, 0)))
    filtered = short_forward(padded_inputs, short_filters)
    product = (filtered[0] * filtered[1]).astype(jnp.bfloat16)
    padded_product = jnp.pad(product, ((filter_len - 1, 0), (0, 0)))
    mix = depthwise(padded_product, medium_filter[::-1]) + skip_gain * product.astype(jnp.float32)
    grad_mix = (weight_seq[:, None] * mix).astype(jnp.bfloat16)
    padded_later = jnp.pad(grad_mix, ((0, filter_len - 1), (0, 0)))
    back_product = depthwise(padded_later, medium_filter) + skip_gain * grad_mix.astype(jnp.float32)
    grad_key = (back_product * filtered[1]).astype(jnp.bfloat16)
    grad_value = (back_product * filtered[0]).astype(jnp.bfloat16)
    grad_filtered = jnp.stack([grad_key, grad_value])
    padded_grads = jnp.pad(grad_filtered, ((0, 0), (0, short_len - 1), (0, 0)))
    grad_channels = short_backward(padded_grads, short_filters).astype(jnp.bfloat16)
    grad_inputs = lax.all_to_all(grad_channels, "ctx", split_axis=1, concat_axis=2, tiled=True)
    grad_taps = depthwise(padded_product, grad_mix)[::-1]
    grad_gain = jnp.sum(grad_mix.astype(jnp.float32) * product.astype(jnp.float32), axis=0)
    grad_short = short_weights(grad_filtered, padded_inputs)
    taps = grad_taps.shape[0]
    stacked = jnp.concatenate(
        [grad_taps, grad_short.reshape(-1, grad_short.shape[-1]), grad_gain[None]], axis=0
    ).astype(jnp.float32)
    stacked = grouped_sum(stacked, "dp", groups, 4)
    grad_taps = stacked[:taps]
    grad_short = stacked[taps : taps + grad_short.shape[0] * short_len].reshape(grad_short.shape)
    grad_gain = stacked[-1]
    return (grad_inputs[:, None], grad_short / groups, grad_taps / groups, grad_gain / groups)


def solution(mesh):
    placed = (
        P(None, "dp", "ctx", None),
        P("dp", "ctx"),
        P(None, None, "ctx"),
        P(None, "ctx"),
        P("ctx"),
    )
    return jax.shard_map(
        local,
        mesh=mesh,
        in_specs=placed,
        out_specs=(P(None, "dp", "ctx", None), P(None, None, "ctx"), P(None, "ctx"), P("ctx")),
        check_vma=False,
    )
```

```python
import jax
import jax.numpy as jnp
from jax import lax
from jax.sharding import PartitionSpec as P


def short_forward(extended, filters):
    short_len = filters.shape[1]
    length = extended.shape[1] - short_len + 1
    result = jnp.zeros((extended.shape[0], length, extended.shape[2]), jnp.float32)
    for offset in range(short_len):
        start = short_len - 1 - offset
        result = result + filters[:, offset][:, None, :] * extended[
            :, start : start + length
        ].astype(jnp.float32)
    return result


def short_backward(extended, filters):
    short_len = filters.shape[1]
    length = extended.shape[1] - short_len + 1
    result = jnp.zeros((extended.shape[0], length, extended.shape[2]), jnp.float32)
    for offset in range(short_len):
        result = result + filters[:, offset][:, None, :] * extended[
            :, offset : offset + length
        ].astype(jnp.float32)
    return result


def short_weights(grads, extended):
    short_len = extended.shape[1] - grads.shape[1] + 1
    length = grads.shape[1]
    rows = []
    for offset in range(short_len):
        start = short_len - 1 - offset
        rows.append(
            jnp.sum(
                grads.astype(jnp.float32) * extended[:, start : start + length].astype(jnp.float32),
                axis=1,
            )
        )
    return jnp.stack(rows, axis=1)


def depthwise(extended, kernel):
    result = lax.conv_general_dilated(
        extended[None],
        kernel[:, None, :],
        (1,),
        "VALID",
        dimension_numbers=("NWC", "WIO", "NWC"),
        feature_group_count=extended.shape[1],
        preferred_element_type=jnp.float32,
    )
    return result[0]


def butterfly_sum(value, axis, size):
    bit = 1
    while bit < size:
        perm = [(i, i ^ bit) for i in range(size)]
        value = value + lax.ppermute(value, axis, perm)
        bit *= 2
    return value


def half_path(inputs, weight_seq, short_filters, medium_filter, skip_gain):
    short_len = short_filters.shape[1]
    filter_len = medium_filter.shape[0]
    all_inputs = lax.all_to_all(inputs, "ctx", split_axis=2, concat_axis=1, tiled=True)
    padded_inputs = jnp.pad(all_inputs, ((0, 0), (short_len - 1, 0), (0, 0)))
    filtered = short_forward(padded_inputs, short_filters)
    product = (filtered[0] * filtered[1]).astype(jnp.bfloat16)
    padded_product = jnp.pad(product, ((filter_len - 1, 0), (0, 0)))
    mix = depthwise(padded_product, medium_filter[::-1]) + skip_gain * product.astype(jnp.float32)
    grad_mix = (weight_seq[:, None] * mix).astype(jnp.bfloat16)
    padded_later = jnp.pad(grad_mix, ((0, filter_len - 1), (0, 0)))
    back_product = depthwise(padded_later, medium_filter) + skip_gain * grad_mix.astype(jnp.float32)
    grad_key = (back_product * filtered[1]).astype(jnp.bfloat16)
    grad_value = (back_product * filtered[0]).astype(jnp.bfloat16)
    grad_filtered = jnp.stack([grad_key, grad_value])
    padded_grads = jnp.pad(grad_filtered, ((0, 0), (0, short_len - 1), (0, 0)))
    grad_channels = short_backward(padded_grads, short_filters).astype(jnp.bfloat16)
    grad_inputs = lax.all_to_all(grad_channels, "ctx", split_axis=1, concat_axis=2, tiled=True)
    grad_taps = depthwise(padded_product, grad_mix)[::-1]
    grad_gain = jnp.sum(grad_mix.astype(jnp.float32) * product.astype(jnp.float32), axis=0)
    grad_short = short_weights(grad_filtered, padded_inputs)
    return grad_inputs, grad_short, grad_taps, grad_gain


def local(projected, token_ids, short_filters, medium_filter, skip_gain):
    inputs = projected[:, 0]
    short_len = short_filters.shape[1]
    length = inputs.shape[1]
    groups = lax.axis_size("dp")
    shards = lax.axis_size("ctx")
    loss_weight = jnp.where((token_ids[0] >= 97) & (token_ids[0] <= 122), 0.1, 1.0).astype(
        jnp.bfloat16
    )
    weight_rows = jnp.broadcast_to(loss_weight[None, :, None], (1, length, shards))
    all_weight = lax.all_to_all(weight_rows, "ctx", split_axis=2, concat_axis=1, tiled=True)
    weight_seq = all_weight[0, :, 0].astype(jnp.float32)
    halves = 2
    width = short_filters.shape[2] // halves
    split_inputs = inputs.reshape(2, length, shards, halves, width)
    results = []
    for h in range(halves):
        cols = slice(h * width, (h + 1) * width)
        part = split_inputs[:, :, :, h].reshape(2, length, shards * width)
        results.append(
            half_path(part, weight_seq, short_filters[:, :, cols], medium_filter[:, cols], skip_gain[cols])
        )
    grad_inputs = jnp.stack(
        [r[0].reshape(2, length, shards, width) for r in results], axis=3
    ).reshape(inputs.shape)
    grad_short = jnp.concatenate([r[1] for r in results], axis=2)
    grad_taps = jnp.concatenate([r[2] for r in results], axis=1)
    grad_gain = jnp.concatenate([r[3] for r in results], axis=0)
    taps = grad_taps.shape[0]
    stacked = jnp.concatenate(
        [grad_taps, grad_short.reshape(-1, grad_short.shape[-1]), grad_gain[None]], axis=0
    ).astype(jnp.float32)
    stacked = butterfly_sum(stacked, "dp", groups)
    grad_taps = stacked[:taps]
    grad_short = stacked[taps : taps + grad_short.shape[0] * short_len].reshape(grad_short.shape)
    grad_gain = stacked[-1]
    return (grad_inputs[:, None], grad_short / groups, grad_taps / groups, grad_gain / groups)


def solution(mesh):
    placed = (
        P(None, "dp", "ctx", None),
        P("dp", "ctx"),
        P(None, None, "ctx"),
        P(None, "ctx"),
        P("ctx"),
    )
    return jax.shard_map(
        local,
        mesh=mesh,
        in_specs=placed,
        out_specs=(P(None, "dp", "ctx", None), P(None, None, "ctx"), P(None, "ctx"), P("ctx")),
        check_vma=False,
    )
```

```python
import jax
import jax.numpy as jnp
from jax import lax
from jax.sharding import PartitionSpec as P


def short_forward(extended, filters):
    short_len = filters.shape[1]
    length = extended.shape[1] - short_len + 1
    result = jnp.zeros((extended.shape[0], length, extended.shape[2]), jnp.float32)
    for offset in range(short_len):
        start = short_len - 1 - offset
        result = result + filters[:, offset][:, None, :] * extended[
            :, start : start + length
        ].astype(jnp.float32)
    return result


def short_backward(extended, filters):
    short_len = filters.shape[1]
    length = extended.shape[1] - short_len + 1
    result = jnp.zeros((extended.shape[0], length, extended.shape[2]), jnp.float32)
    for offset in range(short_len):
        result = result + filters[:, offset][:, None, :] * extended[
            :, offset : offset + length
        ].astype(jnp.float32)
    return result


def short_weights(grads, extended):
    short_len = extended.shape[1] - grads.shape[1] + 1
    length = grads.shape[1]
    rows = []
    for offset in range(short_len):
        start = short_len - 1 - offset
        rows.append(
            jnp.sum(
                grads.astype(jnp.float32) * extended[:, start : start + length].astype(jnp.float32),
                axis=1,
            )
        )
    return jnp.stack(rows, axis=1)


def depthwise(extended, kernel):
    lanes = 128
    if extended.shape[1] > lanes and extended.shape[1] % lanes == 0:
        return jnp.concatenate(
            [
                depthwise(extended[:, k : k + lanes], kernel[:, k : k + lanes])
                for k in range(0, extended.shape[1], lanes)
            ],
            axis=1,
        )
    result = lax.conv_general_dilated(
        extended[None],
        kernel[:, None, :],
        (1,),
        "VALID",
        dimension_numbers=("NWC", "WIO", "NWC"),
        feature_group_count=extended.shape[1],
        preferred_element_type=jnp.float32,
    )
    return result[0]


def butterfly_sum(value, axis, size):
    bit = 1
    while bit < size:
        perm = [(i, i ^ bit) for i in range(size)]
        value = value + lax.ppermute(value, axis, perm)
        bit *= 2
    return value


def local(projected, token_ids, short_filters, medium_filter, skip_gain):
    inputs = projected[:, 0]
    short_len = short_filters.shape[1]
    filter_len = medium_filter.shape[0]
    length = inputs.shape[1]
    groups = lax.axis_size("dp")
    shards = lax.axis_size("ctx")
    loss_weight = jnp.where((token_ids[0] >= 97) & (token_ids[0] <= 122), 0.1, 1.0).astype(
        jnp.bfloat16
    )
    weight_rows = jnp.broadcast_to(loss_weight[None, :, None], (1, length, shards))
    all_inputs, all_weight = (
        lax.all_to_all(inputs, "ctx", split_axis=2, concat_axis=1, tiled=True),
        lax.all_to_all(weight_rows, "ctx", split_axis=2, concat_axis=1, tiled=True),
    )
    weight_seq = all_weight[0, :, 0].astype(jnp.float32)
    padded_inputs = jnp.pad(all_inputs, ((0, 0), (short_len - 1, 0), (0, 0)))
    filtered = short_forward(padded_inputs, short_filters)
    product = (filtered[0] * filtered[1]).astype(jnp.bfloat16)
    padded_product = jnp.pad(product, ((filter_len - 1, 0), (0, 0)))
    mix = depthwise(padded_product, medium_filter[::-1]) + skip_gain * product.astype(jnp.float32)
    grad_mix = (weight_seq[:, None] * mix).astype(jnp.bfloat16)
    padded_later = jnp.pad(grad_mix, ((0, filter_len - 1), (0, 0)))
    back_product = depthwise(padded_later, medium_filter) + skip_gain * grad_mix.astype(jnp.float32)
    grad_key = (back_product * filtered[1]).astype(jnp.bfloat16)
    grad_value = (back_product * filtered[0]).astype(jnp.bfloat16)
    grad_filtered = jnp.stack([grad_key, grad_value])
    padded_grads = jnp.pad(grad_filtered, ((0, 0), (0, short_len - 1), (0, 0)))
    grad_channels = short_backward(padded_grads, short_filters).astype(jnp.bfloat16)
    grad_inputs = lax.all_to_all(grad_channels, "ctx", split_axis=1, concat_axis=2, tiled=True)
    grad_taps = depthwise(padded_product, grad_mix)[::-1]
    grad_gain = jnp.sum(grad_mix.astype(jnp.float32) * product.astype(jnp.float32), axis=0)
    grad_short = short_weights(grad_filtered, padded_inputs)
    taps = grad_taps.shape[0]
    stacked = jnp.concatenate(
        [grad_taps, grad_short.reshape(-1, grad_short.shape[-1]), grad_gain[None]], axis=0
    ).astype(jnp.float32)
    stacked = butterfly_sum(stacked, "dp", groups)
    grad_taps = stacked[:taps]
    grad_short = stacked[taps : taps + grad_short.shape[0] * short_len].reshape(grad_short.shape)
    grad_gain = stacked[-1]
    return (grad_inputs[:, None], grad_short / groups, grad_taps / groups, grad_gain / groups)


def solution(mesh):
    placed = (
        P(None, "dp", "ctx", None),
        P("dp", "ctx"),
        P(None, None, "ctx"),
        P(None, "ctx"),
        P("ctx"),
    )
    return jax.shard_map(
        local,
        mesh=mesh,
        in_specs=placed,
        out_specs=(P(None, "dp", "ctx", None), P(None, None, "ctx"), P(None, "ctx"), P("ctx")),
        check_vma=False,
    )
```

```python
import jax
import jax.numpy as jnp
from jax import lax
from jax.sharding import PartitionSpec as P


def short_forward(extended, filters):
    short_len = filters.shape[1]
    length = extended.shape[1] - short_len + 1
    result = jnp.zeros((extended.shape[0], length, extended.shape[2]), jnp.float32)
    for offset in range(short_len):
        start = short_len - 1 - offset
        result = result + filters[:, offset][:, None, :] * extended[
            :, start : start + length
        ].astype(jnp.float32)
    return result


def short_backward(extended, filters):
    short_len = filters.shape[1]
    length = extended.shape[1] - short_len + 1
    result = jnp.zeros((extended.shape[0], length, extended.shape[2]), jnp.float32)
    for offset in range(short_len):
        result = result + filters[:, offset][:, None, :] * extended[
            :, offset : offset + length
        ].astype(jnp.float32)
    return result


def short_weights(grads, extended):
    short_len = extended.shape[1] - grads.shape[1] + 1
    length = grads.shape[1]
    rows = []
    for offset in range(short_len):
        start = short_len - 1 - offset
        rows.append(
            jnp.sum(
                grads.astype(jnp.float32) * extended[:, start : start + length].astype(jnp.float32),
                axis=1,
            )
        )
    return jnp.stack(rows, axis=1)


def depthwise(extended, kernel):
    lanes = 128
    if extended.shape[1] > lanes and extended.shape[1] % lanes == 0:
        return jnp.concatenate(
            [
                depthwise(extended[:, k : k + lanes], kernel[:, k : k + lanes])
                for k in range(0, extended.shape[1], lanes)
            ],
            axis=1,
        )
    result = lax.conv_general_dilated(
        extended[None],
        kernel[:, None, :],
        (1,),
        "VALID",
        dimension_numbers=("NWC", "WIO", "NWC"),
        feature_group_count=extended.shape[1],
        preferred_element_type=jnp.float32,
    )
    return result[0]


def butterfly_sum(value, axis, size):
    bit = 1
    while bit < size:
        perm = [(i, i ^ bit) for i in range(size)]
        value = value + lax.ppermute(value, axis, perm)
        bit *= 2
    return value


def local(projected, token_ids, short_filters, medium_filter, skip_gain):
    inputs = projected[:, 0]
    short_len = short_filters.shape[1]
    filter_len = medium_filter.shape[0]
    length = inputs.shape[1]
    groups = lax.axis_size("dp")
    shards = lax.axis_size("ctx")
    loss_weight = jnp.where((token_ids[0] >= 97) & (token_ids[0] <= 122), 0.1, 1.0).astype(
        jnp.bfloat16
    )
    weight_rows = jnp.broadcast_to(loss_weight[None, :, None], (1, length, shards))
    all_inputs, all_weight = (
        lax.all_to_all(inputs, "ctx", split_axis=2, concat_axis=1, tiled=True),
        lax.all_to_all(weight_rows, "ctx", split_axis=2, concat_axis=1, tiled=True),
    )
    weight_seq = all_weight[0, :, 0].astype(jnp.float32)
    padded_inputs = jnp.pad(all_inputs, ((0, 0), (short_len - 1, 0), (0, 0)))
    filtered = short_forward(padded_inputs, short_filters)
    product = (filtered[0] * filtered[1]).astype(jnp.bfloat16)
    padded_product = jnp.pad(product, ((filter_len - 1, 0), (0, 0)))
    mix = depthwise(padded_product, medium_filter[::-1]) + skip_gain * product.astype(jnp.float32)
    grad_mix = (weight_seq[:, None] * mix).astype(jnp.bfloat16)
    padded_later = jnp.pad(grad_mix, ((0, filter_len - 1), (0, 0)))
    back_product = depthwise(padded_later, medium_filter) + skip_gain * grad_mix.astype(jnp.float32)
    grad_key = (back_product * filtered[1]).astype(jnp.bfloat16)
    grad_value = (back_product * filtered[0]).astype(jnp.bfloat16)
    grad_filtered = jnp.stack([grad_key, grad_value])
    padded_grads = jnp.pad(grad_filtered, ((0, 0), (0, short_len - 1), (0, 0)))
    grad_channels = short_backward(padded_grads, short_filters).astype(jnp.bfloat16)
    grad_taps = depthwise(padded_product, grad_mix)[::-1]
    grad_gain = jnp.sum(grad_mix.astype(jnp.float32) * product.astype(jnp.float32), axis=0)
    grad_short = short_weights(grad_filtered, padded_inputs)
    taps = grad_taps.shape[0]
    stacked = jnp.concatenate(
        [grad_taps, grad_short.reshape(-1, grad_short.shape[-1]), grad_gain[None]], axis=0
    ).astype(jnp.float32)
    stacked = butterfly_sum(stacked, "dp", groups)
    stacked, grad_channels = lax.optimization_barrier((stacked, grad_channels))
    grad_inputs = lax.all_to_all(grad_channels, "ctx", split_axis=1, concat_axis=2, tiled=True)
    grad_taps = stacked[:taps]
    grad_short = stacked[taps : taps + grad_short.shape[0] * short_len].reshape(grad_short.shape)
    grad_gain = stacked[-1]
    return (grad_inputs[:, None], grad_short / groups, grad_taps / groups, grad_gain / groups)


def solution(mesh):
    placed = (
        P(None, "dp", "ctx", None),
        P("dp", "ctx"),
        P(None, None, "ctx"),
        P(None, "ctx"),
        P("ctx"),
    )
    return jax.shard_map(
        local,
        mesh=mesh,
        in_specs=placed,
        out_specs=(P(None, "dp", "ctx", None), P(None, None, "ctx"), P(None, "ctx"), P("ctx")),
        check_vma=False,
    )
```

```python
import jax
import jax.numpy as jnp
from jax import lax
from jax.sharding import PartitionSpec as P


def short_forward(extended, filters):
    short_len = filters.shape[1]
    length = extended.shape[1] - short_len + 1
    result = jnp.zeros((extended.shape[0], length, extended.shape[2]), jnp.float32)
    for offset in range(short_len):
        start = short_len - 1 - offset
        result = result + filters[:, offset][:, None, :] * extended[
            :, start : start + length
        ].astype(jnp.float32)
    return result


def short_backward(extended, filters):
    short_len = filters.shape[1]
    length = extended.shape[1] - short_len + 1
    result = jnp.zeros((extended.shape[0], length, extended.shape[2]), jnp.float32)
    for offset in range(short_len):
        result = result + filters[:, offset][:, None, :] * extended[
            :, offset : offset + length
        ].astype(jnp.float32)
    return result


def short_weights(grads, extended):
    short_len = extended.shape[1] - grads.shape[1] + 1
    length = grads.shape[1]
    rows = []
    for offset in range(short_len):
        start = short_len - 1 - offset
        rows.append(
            jnp.sum(
                grads.astype(jnp.float32) * extended[:, start : start + length].astype(jnp.float32),
                axis=1,
            )
        )
    return jnp.stack(rows, axis=1)


def depthwise(extended, kernel):
    lanes = 128
    if extended.shape[1] > lanes and extended.shape[1] % lanes == 0:
        return jnp.concatenate(
            [
                depthwise(extended[:, k : k + lanes], kernel[:, k : k + lanes])
                for k in range(0, extended.shape[1], lanes)
            ],
            axis=1,
        )
    result = lax.conv_general_dilated(
        extended[None],
        kernel[:, None, :],
        (1,),
        "VALID",
        dimension_numbers=("NWC", "WIO", "NWC"),
        feature_group_count=extended.shape[1],
        preferred_element_type=jnp.float32,
    )
    return result[0]


def butterfly_sum(value, axis, size):
    bit = 1
    while bit < size:
        perm = [(i, i ^ bit) for i in range(size)]
        value = value.astype(jnp.bfloat16)
        value = value.astype(jnp.float32) + lax.ppermute(value, axis, perm).astype(jnp.float32)
        bit *= 2
    return value


def local(projected, token_ids, short_filters, medium_filter, skip_gain):
    inputs = projected[:, 0]
    short_len = short_filters.shape[1]
    filter_len = medium_filter.shape[0]
    length = inputs.shape[1]
    groups = lax.axis_size("dp")
    shards = lax.axis_size("ctx")
    loss_weight = jnp.where((token_ids[0] >= 97) & (token_ids[0] <= 122), 0.1, 1.0).astype(
        jnp.bfloat16
    )
    weight_rows = jnp.broadcast_to(loss_weight[None, :, None], (1, length, shards))
    all_inputs, all_weight = (
        lax.all_to_all(inputs, "ctx", split_axis=2, concat_axis=1, tiled=True),
        lax.all_to_all(weight_rows, "ctx", split_axis=2, concat_axis=1, tiled=True),
    )
    weight_seq = all_weight[0, :, 0].astype(jnp.float32)
    padded_inputs = jnp.pad(all_inputs, ((0, 0), (short_len - 1, 0), (0, 0)))
    filtered = short_forward(padded_inputs, short_filters)
    product = (filtered[0] * filtered[1]).astype(jnp.bfloat16)
    padded_product = jnp.pad(product, ((filter_len - 1, 0), (0, 0)))
    mix = depthwise(padded_product, medium_filter[::-1]) + skip_gain * product.astype(jnp.float32)
    grad_mix = (weight_seq[:, None] * mix).astype(jnp.bfloat16)
    padded_later = jnp.pad(grad_mix, ((0, filter_len - 1), (0, 0)))
    back_product = depthwise(padded_later, medium_filter) + skip_gain * grad_mix.astype(jnp.float32)
    grad_key = (back_product * filtered[1]).astype(jnp.bfloat16)
    grad_value = (back_product * filtered[0]).astype(jnp.bfloat16)
    grad_filtered = jnp.stack([grad_key, grad_value])
    padded_grads = jnp.pad(grad_filtered, ((0, 0), (0, short_len - 1), (0, 0)))
    grad_channels = short_backward(padded_grads, short_filters).astype(jnp.bfloat16)
    grad_inputs = lax.all_to_all(grad_channels, "ctx", split_axis=1, concat_axis=2, tiled=True)
    grad_taps = depthwise(padded_product, grad_mix)[::-1]
    grad_gain = jnp.sum(grad_mix.astype(jnp.float32) * product.astype(jnp.float32), axis=0)
    grad_short = short_weights(grad_filtered, padded_inputs)
    taps = grad_taps.shape[0]
    stacked = jnp.concatenate(
        [grad_taps, grad_short.reshape(-1, grad_short.shape[-1]), grad_gain[None]], axis=0
    ).astype(jnp.float32)
    stacked = butterfly_sum(stacked, "dp", groups)
    grad_taps = stacked[:taps]
    grad_short = stacked[taps : taps + grad_short.shape[0] * short_len].reshape(grad_short.shape)
    grad_gain = stacked[-1]
    return (grad_inputs[:, None], grad_short / groups, grad_taps / groups, grad_gain / groups)


def solution(mesh):
    placed = (
        P(None, "dp", "ctx", None),
        P("dp", "ctx"),
        P(None, None, "ctx"),
        P(None, "ctx"),
        P("ctx"),
    )
    return jax.shard_map(
        local,
        mesh=mesh,
        in_specs=placed,
        out_specs=(P(None, "dp", "ctx", None), P(None, None, "ctx"), P(None, "ctx"), P("ctx")),
        check_vma=False,
    )
```
